32 devices in a mesh: dp: 2 (over x), seq: 16 (over z, y, core).
Axes of the slice: x: 2, y: 2, z: 4, core: 2. Of those that a mesh axis runs over, the one named last changes fastest.
Arguments:
- tokens: bfloat16 [16384, 1024], P(('dp', 'seq')), may hold values from -6 to 6
- segment_ids: int32 [16384], P('dp'), may hold values from 0 to 7, never falling along the last dimension, each value on 1 to 4096 neighbouring positions
- attn_gain: bfloat16 [1024], replicated, may hold values from 0.099609375 to 1.8984375
- attn_shift: bfloat16 [1024], replicated, may hold values from -3 to 3
- qkv_weight: bfloat16 [1024, 3072], replicated, may hold values from -0.1875 to 0.1875
- query_bias: bfloat16 [1024], replicated, may hold values from -3 to 3
- value_bias: bfloat16 [1024], replicated, may hold values from -3 to 3
- out_weight: bfloat16 [1024, 1024], replicated, may hold values from -0.5 to 0.5
- out_bias: bfloat16 [1024], replicated, may hold values from -3 to 3
- mlp_gain: bfloat16 [1024], replicated, may hold values from 0.099609375 to 1.8984375
- mlp_shift: bfloat16 [1024], replicated, may hold values from -3 to 3
- up_weight: bfloat16 [1024, 4096], replicated, may hold values from -0.1875 to 0.1875
- up_bias: bfloat16 [4096], replicated, may hold values from -3 to 3
- down_weight: bfloat16 [4096, 1024], replicated, may hold values from -0.125 to 0.125
- down_bias: bfloat16 [1024], replicated, may hold values from -3 to 3
- cotangent: bfloat16 [16384, 1024], P(('dp', 'seq')), may hold values from -6 to 6
Outputs:
- output: bfloat16 [16384, 1024], P(('dp', 'seq'))
- grad_tokens: bfloat16 [16384, 1024], P(('dp', 'seq'))
- grad_attn_gain: float32 [1024], P(('dp', 'seq'))
- grad_attn_shift: float32 [1024], P(('dp', 'seq'))
- grad_qkv_weight: float32 [1024, 3072], P(('dp', 'seq'))
- grad_query_bias: float32 [1024], P(('dp', 'seq'))
- grad_value_bias: float32 [1024], P(('dp', 'seq'))
- grad_out_weight: float32 [1024, 1024], P(('dp', 'seq'))
- grad_out_bias: float32 [1024], P(('dp', 'seq'))
- grad_mlp_gain: float32 [1024], P(('dp', 'seq'))
- grad_mlp_shift: float32 [1024], P(('dp', 'seq'))
- grad_up_weight: float32 [1024, 4096], P(('dp', 'seq'))
- grad_up_bias: float32 [4096], P(('dp', 'seq'))
- grad_down_weight: float32 [4096, 1024], P(('dp', 'seq'))
- grad_down_bias: float32 [1024], P(('dp', 'seq'))
The draws below stay inside these ranges and needn't reach their ends.
Inputs may be any that keep to these rules, and one draw needn't show every extreme that they name: `segment_ids`: ids never fall along the tokens; one id covers at most 4096 consecutive tokens, and some id exactly that many.
All inputs are finite; a program needn't handle non-finite values.
Results may differ from the reference program's by a relative error of at most 0.011.
Values may be sent and summed in bfloat16 or wider, within the bound.
No kernel may reach another device: no remote copies, remote signals or barrier semaphores. Data moves between devices by JAX's collectives and lax.ppermute only.
A program may use at most 256 MiB of HBM per device.

```python
import math
import jax
import jax.numpy as jnp
import numpy as np
from jax import lax

D = 1024
HEADS = 16
FF = 4096
BLOCK = 128
WIN_ROWS = 64
TOKENS = 16384
CLIPS = 8
CLIP_MOST = 4096


def spiked(values, own_key, source, target, blocks, factor):
    owner, partner = [(jnp.arange(values.shape[axis_at]) // (values.shape[axis_at] // blocks)).reshape([-1 if axis == axis_at else 1 for axis in range(values.ndim)]) for axis_at in (source, target)]
    chosen = jax.random.permutation(own_key, blocks)[partner]
    strong = (owner == chosen) | (owner == (partner + blocks // 2) % blocks)
    return jnp.where(strong, factor * values, values)


def block_scale(rng, shape, split, smallest, high):
    def one(position, shards_of):
        steps = jax.random.uniform(jax.random.fold_in(jax.random.fold_in(rng, 6), position), (shards_of,), jnp.float32, smallest / len(split), high / len(split))
        return jnp.repeat(jnp.exp(steps), shape[position] // shards_of).reshape((-1,) + (1,) * (len(shape) - position - 1))

    level = one(*split[0])
    for cut in split[1:]:
        level = level * one(*cut)
    return level


def split_up(number_of, total, most, lean):
    portions = [(1 << 20) // math.isqrt(grade ** lean) + 1 for grade in range(2, number_of + 1)]
    surplus, holding = total - most - (number_of - 1), [1] * (number_of - 1)
    while surplus > 0:
        candidates = [i for i in range(number_of - 1) if holding[i] < most]
        pool, left = sum([portions[i] for i in candidates]), surplus
        for i in candidates:
            addition = min(most - holding[i], max(1, left * portions[i] // pool), surplus)
            holding[i] = holding[i] + addition
            surplus = surplus - addition
    return np.array([most] + holding)


def uneven_parts(key, amount, total, limit, lean):
    if amount == 2:
        one = jax.random.randint(key, (), max(1, total - limit), min(limit, total - 1) + 1)
        return jnp.stack([one, total - one])
    tallies = jnp.asarray(split_up(amount, total, limit, lean), jnp.int32)
    twos = (amount - 1) // 2
    donor, sink = tallies[1:1 + 2 * twos:2], tallies[2:2 + 2 * twos:2]
    room = jnp.minimum(donor - 1, limit - sink)
    moved = jax.random.randint(jax.random.fold_in(key, 1), (twos,), 0, 1 << 20) % (room + 1)
    tallies = tallies.at[1:1 + 2 * twos:2].set(donor - moved).at[2:2 + 2 * twos:2].set(sink + moved)
    return tallies[jax.random.permutation(jax.random.fold_in(key, 2), amount)]


def normal_values(own_key, extent, spread, most, split=(), dtype=jnp.bfloat16):
    loudness = block_scale(own_key, extent, split, -0.22, 0.18) if split else 1.0
    values = jax.random.normal(own_key, extent, jnp.float32) * spread * loudness
    return jnp.minimum(jnp.maximum(values, -most), most).astype(dtype)


def bell_draw_with(own_key, dims, scale, reach, pieces, heavy, dtype=jnp.bfloat16):
    values = scale * jax.random.normal(own_key, dims, jnp.float32)
    if pieces:
        values = values * block_scale(own_key, dims, pieces, -0.22, 0.18)
    return jnp.clip(spiked(values, jax.random.fold_in(own_key, 3), *heavy), -reach, reach).astype(dtype)


def setup_inputs(seed: int = 0) -> dict:
    key_of = jax.random.split(jax.random.key(seed), 17)
    tokens = normal_values(key_of[0], (TOKENS, D), 1.0, 6.0, ((0, 32),))
    segment_ids = jnp.searchsorted(jnp.cumsum(uneven_parts(key_of[1], CLIPS, TOKENS, CLIP_MOST, 1)), jnp.arange(TOKENS), side="right").astype(jnp.int32)
    attn_gain = jnp.clip(1.0 + 0.18 * jax.random.normal(key_of[2], (D,), jnp.float32), 0.099609375, 1.8984375).astype(jnp.bfloat16)
    attn_shift = normal_values(key_of[3], (D,), 0.5, 3.0)
    qkv_weight = normal_values(key_of[4], (D, 3 * D), D ** -0.5, 0.1875)
    query_bias = normal_values(key_of[5], (D,), 0.5, 3.0)
    value_bias = normal_values(key_of[6], (D,), 0.5, 3.0)
    out_weight = normal_values(key_of[7], (D, D), (D // 8) ** -0.5, 0.5)
    out_bias = normal_values(key_of[8], (D,), 0.5, 3.0)
    mlp_gain = jnp.clip(1.0 + 0.18 * jax.random.normal(key_of[9], (D,), jnp.float32), 0.099609375, 1.8984375).astype(jnp.bfloat16)
    mlp_shift = normal_values(key_of[10], (D,), 0.5, 3.0)
    up_weight = normal_values(key_of[11], (D, FF), D ** -0.5, 0.1875)
    up_bias = normal_values(key_of[12], (FF,), 0.5, 3.0)
    down_weight = normal_values(key_of[13], (FF, D), (FF // 2) ** -0.5, 0.125)
    down_bias = normal_values(key_of[14], (D,), 0.5, 3.0)
    cotangent = bell_draw_with(key_of[15], (TOKENS, D), 1.0, 6.0, ((0, 32),), (0, 1, 32, 2.75))
    return dict(tokens=tokens, segment_ids=segment_ids, attn_gain=attn_gain, attn_shift=attn_shift, qkv_weight=qkv_weight, query_bias=query_bias, value_bias=value_bias, out_weight=out_weight, out_bias=out_bias, mlp_gain=mlp_gain, mlp_shift=mlp_shift, up_weight=up_weight, up_bias=up_bias, down_weight=down_weight, down_bias=down_bias, cotangent=cotangent)


EPSILON = 1e-05
NEG_FILL = -1e+30
HIGH = lax.Precision.HIGHEST

@jax.custom_vjp
def low(v):
    return lax.optimization_barrier(v.astype(jnp.bfloat16)).astype(jnp.float32)

@jax.custom_vjp
def low_back(v):
    return v

def low_keep(v):
    return (low(v), None)

def low_pass(kept, grad):
    return (grad,)

def back_keep(v):
    return (v, None)

def back_low(kept, grad):
    return (low(grad),)
low.defvjp(low_keep, low_pass)
low_back.defvjp(back_keep, back_low)

def gelu_tanh(values):
    return 0.5 * values * (1.0 + jnp.tanh(0.7978845608028654 * (values + 0.044715 * values * values * values)))

def layer_norm(values, gain, shift):
    center = values - lax.optimization_barrier(jnp.mean(values, axis=-1, keepdims=True))
    scaled = center * lax.rsqrt(lax.optimization_barrier(jnp.mean(center * center, axis=-1, keepdims=True)) + EPSILON)
    return scaled * gain + shift

def window_layer(params, window_tokens, window_segments):
    attn_gain, attn_shift, qkv_weight, query_bias, value_bias, out_weight, out_bias, mlp_gain, mlp_shift, up_weight, up_bias, down_weight, down_bias = params
    width = window_tokens.shape[-1]
    head_dim = width // HEADS
    flat = window_tokens.reshape(-1, width)
    normed = low(layer_norm(flat, attn_gain, attn_shift))
    bias_all = jnp.concatenate([query_bias, jnp.zeros_like(query_bias), value_bias])
    projected = jnp.dot(normed, qkv_weight, precision=HIGH) + bias_all
    projected = low(low_back(projected))
    shaped = projected.reshape(WIN_ROWS, BLOCK, 3, HEADS, head_dim)
    queries = shaped[:, :, 0]
    keys = shaped[:, :, 1]
    values = shaped[:, :, 2]
    raw = jnp.einsum('qchd,kchd->chqk', queries, keys, precision=HIGH)
    logits = low_back(raw * head_dim ** (-0.5))
    row_ids = jnp.arange(WIN_ROWS)
    causal = row_ids[None, :] <= row_ids[:, None]
    seg_cols = window_segments.T
    allowed = (seg_cols[:, :, None] == seg_cols[:, None, :]) & causal[None]
    logits = jnp.where(allowed[:, None], logits, NEG_FILL)
    shifted = jnp.exp(logits - lax.optimization_barrier(jnp.max(logits, axis=-1, keepdims=True)))
    probs = shifted / lax.optimization_barrier(jnp.sum(shifted, axis=-1, keepdims=True))
    attended = jnp.einsum('chqk,kchd->qchd', low(probs), values, precision=HIGH)
    attended = low(low_back(attended)).reshape(-1, width)
    branch = low_back(jnp.dot(attended, out_weight, precision=HIGH) + out_bias)
    middle = flat + branch
    second = low(layer_norm(middle, mlp_gain, mlp_shift))
    hidden = low_back(jnp.dot(second, up_weight, precision=HIGH) + up_bias)
    activated = low(gelu_tanh(hidden))
    mixed = low_back(jnp.dot(activated, down_weight, precision=HIGH) + down_bias)
    return (middle + mixed).reshape(window_tokens.shape)

def reference(tokens, segment_ids, attn_gain, attn_shift, qkv_weight, query_bias, value_bias, out_weight, out_bias, mlp_gain, mlp_shift, up_weight, up_bias, down_weight, down_bias, cotangent):
    params = tuple((item.astype(jnp.float32) for item in (attn_gain, attn_shift, qkv_weight, query_bias, value_bias, out_weight, out_bias, mlp_gain, mlp_shift, up_weight, up_bias, down_weight, down_bias)))
    width = tokens.shape[1]
    windows = tokens.astype(jnp.float32).reshape(-1, WIN_ROWS, BLOCK, width)
    segments = segment_ids.reshape(-1, WIN_ROWS, BLOCK)
    step = jax.checkpoint(window_layer)

    def forward(weights, inputs):
        return lax.map(lambda pair: step(weights, pair[0], pair[1]), (inputs, segments))
    result, pullback = jax.vjp(forward, params, windows)
    weight_grads, token_grads = pullback(cotangent.astype(jnp.float32).reshape(result.shape))
    grad_attn_gain, grad_attn_shift, grad_qkv_weight, grad_query_bias, grad_value_bias, grad_out_weight, grad_out_bias, grad_mlp_gain, grad_mlp_shift, grad_up_weight, grad_up_bias, grad_down_weight, grad_down_bias = weight_grads
    return (result.reshape(-1, width).astype(jnp.bfloat16), token_grads.reshape(-1, width).astype(jnp.bfloat16), grad_attn_gain, grad_attn_shift, grad_qkv_weight, grad_query_bias, grad_value_bias, grad_out_weight, grad_out_bias, grad_mlp_gain, grad_mlp_shift, grad_up_weight, grad_up_bias, grad_down_weight, grad_down_bias)
```

```python
import jax
import jax.numpy as jnp
from jax import lax
from jax.sharding import PartitionSpec as P

HEADS = 16
BLOCK = 128
WIN_ROWS = 64


EPSILON = 1e-05
NEG_FILL = -1e30
WIDE = jnp.float32
NARROW = jnp.bfloat16
AXES = ("dp", "seq")
COLOR_FRACTIONS = (0.5, 0.375, 0.125)


def gelu_tanh(values):
    return (
        0.5
        * values
        * (1.0 + jnp.tanh(0.7978845608028654 * (values + 0.044715 * values * values * values)))
    )


def norm_forward(values, gain, shift):
    center = values - jnp.mean(values, axis=-1, keepdims=True)
    inverse = lax.rsqrt(jnp.mean(center * center, axis=-1, keepdims=True) + EPSILON)
    scaled = center * inverse
    return (scaled * gain + shift, scaled, inverse)


def norm_backward(upstream, gain, scaled, inverse):
    weighted = upstream * gain
    inner = (
        weighted
        - jnp.mean(weighted, axis=-1, keepdims=True)
        - scaled * jnp.mean(weighted * scaled, axis=-1, keepdims=True)
    )
    return (inverse * inner, jnp.sum(upstream * scaled, axis=0), jnp.sum(upstream, axis=0))


def color_orders(bits):
    rest = list(range(1, bits))
    if not rest:
        return [[0]]
    starts = [len(rest) - 1, 0, 1]
    return [[0] + rest[s % len(rest):] + rest[: s % len(rest)] for s in starts]


def halving(part, order, me, count):
    bits = len(order)
    rows, cols = part.shape
    buf = part.reshape((2,) * bits + (rows // count, cols))
    left = list(range(bits - 1, -1, -1))
    for bit in order:
        axis = left.index(bit)
        mine = (me >> bit) & 1
        keep = lax.dynamic_index_in_dim(buf, mine, axis, keepdims=False)
        send = lax.dynamic_index_in_dim(buf, 1 - mine, axis, keepdims=False).astype(NARROW)
        got = lax.ppermute(send, AXES, [(i, i ^ (1 << bit)) for i in range(count)])
        buf = keep.astype(WIDE) + got.astype(WIDE)
        left.pop(axis)
    return buf.reshape(rows // count, cols)


def color_cuts(cols):
    cuts = [0]
    for fraction in COLOR_FRACTIONS[:-1]:
        cuts.append(cuts[-1] + max(128, int(round(cols * fraction / 128)) * 128))
    cuts.append(cols)
    return cuts


def reduced_weight(lhs, rhs, me, count, orders):
    cols = rhs.shape[1]
    cuts = color_cuts(cols)
    pieces = []
    for a, b, order in zip(cuts[:-1], cuts[1:], orders):
        partial = jnp.einsum("tr,tc->rc", lhs, rhs[:, a:b], preferred_element_type=WIDE)
        pieces.append(halving(partial, order, me, count))
    return jnp.concatenate(pieces, axis=1)


def per_device(
    tokens,
    segment_ids,
    attn_gain,
    attn_shift,
    qkv_weight,
    query_bias,
    value_bias,
    out_weight,
    out_bias,
    mlp_gain,
    mlp_shift,
    up_weight,
    up_bias,
    down_weight,
    down_bias,
    cotangent,
):
    width = tokens.shape[1]
    head_dim = width // HEADS
    scale = head_dim ** (-0.5)
    seq_count = lax.axis_size("seq")
    count = lax.axis_size("dp") * seq_count
    bits = count.bit_length() - 1
    me = lax.axis_index("dp") * seq_count + lax.axis_index("seq")
    orders = color_orders(bits)
    local_rows = tokens.shape[0] // BLOCK
    all_rows = local_rows * seq_count
    columns = BLOCK // seq_count
    windows = all_rows // WIN_ROWS

    def to_columns(rows_array):
        w = rows_array.shape[-1]
        shaped = rows_array.reshape(local_rows, BLOCK, w)
        moved = lax.all_to_all(shaped, "seq", split_axis=1, concat_axis=0, tiled=True)
        return moved.reshape(all_rows * columns, w)

    def to_rows(column_array):
        w = column_array.shape[-1]
        shaped = column_array.reshape(all_rows, columns, w)
        moved = lax.all_to_all(shaped, "seq", split_axis=0, concat_axis=1, tiled=True)
        return moved.reshape(local_rows * BLOCK, w)

    def heads(flat):
        return flat.reshape(windows, WIN_ROWS, columns, HEADS, head_dim)

    gain_first = attn_gain.astype(WIDE)
    shift_first = attn_shift.astype(WIDE)
    gain_second = mlp_gain.astype(WIDE)
    shift_second = mlp_shift.astype(WIDE)

    tokens_col = to_columns(tokens)
    cotangent_col = to_columns(cotangent)

    group_segments = segment_ids.reshape(all_rows, BLOCK)
    my_segments = lax.dynamic_slice_in_dim(
        group_segments, lax.axis_index("seq") * columns, columns, 1
    )
    seg = jnp.transpose(my_segments.reshape(windows, WIN_ROWS, columns), (0, 2, 1))
    row_ids = jnp.arange(WIN_ROWS)
    causal = row_ids[None, :] <= row_ids[:, None]
    allowed = (seg[:, :, :, None] == seg[:, :, None, :]) & causal
    allowed = allowed[:, :, None]

    residual = tokens_col.astype(WIDE)
    first, first_scaled, first_inverse = norm_forward(residual, gain_first, shift_first)
    first_low = first.astype(NARROW)
    bias_all = jnp.concatenate(
        [query_bias.astype(WIDE), jnp.zeros((width,), WIDE), value_bias.astype(WIDE)]
    )
    projected = (jnp.dot(first_low, qkv_weight, preferred_element_type=WIDE) + bias_all).astype(
        NARROW
    )
    queries = heads(projected[:, :width])
    keys = heads(projected[:, width : 2 * width])
    values = heads(projected[:, 2 * width :])
    raw = jnp.einsum("wqchd,wkchd->wchqk", queries, keys, preferred_element_type=WIDE)
    logits = jnp.where(allowed, raw * scale, NEG_FILL)
    peak = jnp.max(logits, axis=-1, keepdims=True)
    total = jnp.sum(jnp.exp(logits - peak), axis=-1, keepdims=True)
    log_total = peak + jnp.log(total)
    probs = jnp.exp(logits - log_total)
    probs_low = probs.astype(NARROW)
    attended = jnp.einsum("wchqk,wkchd->wqchd", probs_low, values, preferred_element_type=WIDE)
    attended = attended.astype(NARROW).reshape(-1, width)
    branch = jnp.dot(attended, out_weight, preferred_element_type=WIDE) + out_bias.astype(WIDE)
    middle = residual + branch
    second, second_scaled, second_inverse = norm_forward(middle, gain_second, shift_second)
    second_low = second.astype(NARROW)
    hidden = jnp.dot(second_low, up_weight, preferred_element_type=WIDE) + up_bias.astype(WIDE)
    activated, gelu_pull = jax.vjp(gelu_tanh, hidden)
    activated_low = activated.astype(NARROW)
    mixed = jnp.dot(activated_low, down_weight, preferred_element_type=WIDE) + down_bias.astype(
        WIDE
    )
    output = to_rows((middle + mixed).astype(NARROW))

    grad_out = cotangent_col.astype(WIDE)
    grad_down_weight = reduced_weight(activated_low, cotangent_col, me, count, orders)
    grad_down_bias = jnp.sum(grad_out, axis=0)
    grad_activated = jnp.einsum(
        "td,fd->tf", cotangent_col, down_weight, preferred_element_type=WIDE
    )
    grad_hidden = gelu_pull(grad_activated)[0].astype(NARROW)
    grad_up_weight = reduced_weight(second_low, grad_hidden, me, count, orders)
    grad_up_bias = jnp.sum(grad_hidden, axis=0, dtype=WIDE)
    grad_second = jnp.einsum("tf,df->td", grad_hidden, up_weight, preferred_element_type=WIDE)
    grad_middle_norm, grad_mlp_gain, grad_mlp_shift = norm_backward(
        grad_second, gain_second, second_scaled, second_inverse
    )
    grad_middle = grad_out + grad_middle_norm
    grad_branch = grad_middle.astype(NARROW)
    grad_out_weight = reduced_weight(attended, grad_branch, me, count, orders)
    grad_out_bias = jnp.sum(grad_branch, axis=0, dtype=WIDE)
    grad_attended = jnp.einsum("te,de->td", grad_branch, out_weight, preferred_element_type=WIDE)
    grad_heads = heads(grad_attended.astype(NARROW))
    grad_values = jnp.einsum(
        "wchqk,wqchd->wkchd", probs_low, grad_heads, preferred_element_type=WIDE
    )
    grad_probs = jnp.einsum("wqchd,wkchd->wchqk", grad_heads, values, preferred_element_type=WIDE)
    grad_logits = (
        probs * (grad_probs - jnp.sum(probs * grad_probs, axis=-1, keepdims=True))
    ).astype(NARROW)
    grad_queries = (
        jnp.einsum("wchqk,wkchd->wqchd", grad_logits, keys, preferred_element_type=WIDE) * scale
    )
    grad_keys = (
        jnp.einsum("wchqk,wqchd->wkchd", grad_logits, queries, preferred_element_type=WIDE) * scale
    )
    grad_projected = jnp.concatenate(
        [
            grad_queries.astype(NARROW).reshape(-1, width),
            grad_keys.astype(NARROW).reshape(-1, width),
            grad_values.astype(NARROW).reshape(-1, width),
        ],
        axis=-1,
    )
    grad_qkv_weight = reduced_weight(first_low, grad_projected, me, count, orders)
    grad_query_bias = jnp.sum(grad_projected[:, :width], axis=0, dtype=WIDE)
    grad_value_bias = jnp.sum(grad_projected[:, 2 * width :], axis=0, dtype=WIDE)
    grad_first = jnp.einsum("te,de->td", grad_projected, qkv_weight, preferred_element_type=WIDE)
    grad_token_norm, grad_attn_gain, grad_attn_shift = norm_backward(
        grad_first, gain_first, first_scaled, first_inverse
    )
    grad_tokens = to_rows((grad_middle + grad_token_norm).astype(NARROW))

    vectors = (
        grad_attn_gain,
        grad_attn_shift,
        grad_query_bias,
        grad_value_bias,
        grad_out_bias,
        grad_mlp_gain,
        grad_mlp_shift,
        grad_up_bias,
        grad_down_bias,
    )
    packed = jnp.concatenate([v.reshape(count, -1) for v in vectors], axis=1)
    summed = halving(packed, orders[1], me, count)
    cuts = [0]
    for v in vectors:
        cuts.append(cuts[-1] + v.shape[0] // count)
    (
        grad_attn_gain,
        grad_attn_shift,
        grad_query_bias,
        grad_value_bias,
        grad_out_bias,
        grad_mlp_gain,
        grad_mlp_shift,
        grad_up_bias,
        grad_down_bias,
    ) = [summed[0, a:b] for a, b in zip(cuts[:-1], cuts[1:])]
    return (
        output,
        grad_tokens,
        grad_attn_gain,
        grad_attn_shift,
        grad_qkv_weight,
        grad_query_bias,
        grad_value_bias,
        grad_out_weight,
        grad_out_bias,
        grad_mlp_gain,
        grad_mlp_shift,
        grad_up_weight,
        grad_up_bias,
        grad_down_weight,
        grad_down_bias,
    )


def solution(mesh):
    placed = (
        P(("dp", "seq"), None),
        P("dp"),
        P(),
        P(),
        P(),
        P(),
        P(),
        P(),
        P(),
        P(),
        P(),
        P(),
        P(),
        P(),
        P(),
        P(("dp", "seq"), None),
    )
    return jax.shard_map(
        per_device,
        mesh=mesh,
        in_specs=placed,
        out_specs=(
            P(("dp", "seq"), None),
            P(("dp", "seq"), None),
            P(("dp", "seq")),
            P(("dp", "seq")),
            P(("dp", "seq"), None),
            P(("dp", "seq")),
            P(("dp", "seq")),
            P(("dp", "seq"), None),
            P(("dp", "seq")),
            P(("dp", "seq")),
            P(("dp", "seq")),
            P(("dp", "seq"), None),
            P(("dp", "seq")),
            P(("dp", "seq"), None),
            P(("dp", "seq")),
        ),
        check_vma=False,
    )
```

```python
import jax
import jax.numpy as jnp
from jax import lax
from jax.sharding import PartitionSpec as P


HEADS = 16
BLOCK = 128
WIN_ROWS = 64


EPSILON = 1e-05
NEG_FILL = -1e30
WIDE = jnp.float32
NARROW = jnp.bfloat16
AXES = ("dp", "seq")
COLOR_FRACTIONS = (0.5, 0.375, 0.125)


def gelu_tanh(values):
    return (
        0.5
        * values
        * (1.0 + jnp.tanh(0.7978845608028654 * (values + 0.044715 * values * values * values)))
    )


def norm_forward(values, gain, shift):
    center = values - jnp.mean(values, axis=-1, keepdims=True)
    inverse = lax.rsqrt(jnp.mean(center * center, axis=-1, keepdims=True) + EPSILON)
    scaled = center * inverse
    return (scaled * gain + shift, scaled, inverse)


def norm_backward(upstream, gain, scaled, inverse):
    weighted = upstream * gain
    inner = (
        weighted
        - jnp.mean(weighted, axis=-1, keepdims=True)
        - scaled * jnp.mean(weighted * scaled, axis=-1, keepdims=True)
    )
    return (inverse * inner, jnp.sum(upstream * scaled, axis=0), jnp.sum(upstream, axis=0))


def color_orders(bits):
    rest = list(range(1, bits))
    if not rest:
        return [[0]]
    starts = [len(rest) - 1, 0, 1]
    return [[0] + rest[s % len(rest):] + rest[: s % len(rest)] for s in starts]


def halving(part, order, me, count):
    bits = len(order)
    rows, cols = part.shape
    buf = part.reshape((2,) * bits + (rows // count, cols))
    left = list(range(bits - 1, -1, -1))
    for bit in order:
        axis = left.index(bit)
        mine = (me >> bit) & 1
        keep = lax.dynamic_index_in_dim(buf, mine, axis, keepdims=False)
        send = lax.dynamic_index_in_dim(buf, 1 - mine, axis, keepdims=False).astype(NARROW)
        got = lax.ppermute(send, AXES, [(i, i ^ (1 << bit)) for i in range(count)])
        buf = keep.astype(WIDE) + got.astype(WIDE)
        left.pop(axis)
    return buf.reshape(rows // count, cols)


def color_cuts(cols):
    cuts = [0]
    for fraction in COLOR_FRACTIONS[:-1]:
        cuts.append(cuts[-1] + max(128, int(round(cols * fraction / 128)) * 128))
    cuts.append(cols)
    return cuts


def reduced_weight(lhs, rhs, me, count, orders):
    cols = rhs.shape[1]
    cuts = color_cuts(cols) if len(orders) > 1 else [0, cols]
    pieces = []
    for a, b, order in zip(cuts[:-1], cuts[1:], orders):
        partial = jnp.einsum("tr,tc->rc", lhs, rhs[:, a:b], preferred_element_type=WIDE)
        pieces.append(halving(partial, order, me, count))
    return pieces[0] if len(pieces) == 1 else jnp.concatenate(pieces, axis=1)


def layer_body(
    tokens,
    segment_ids,
    attn_gain,
    attn_shift,
    qkv_weight,
    query_bias,
    value_bias,
    out_weight,
    out_bias,
    mlp_gain,
    mlp_shift,
    up_weight,
    up_bias,
    down_weight,
    down_bias,
    cotangent,
):
    width = tokens.shape[1]
    head_dim = width // HEADS
    scale = head_dim ** (-0.5)
    seq_count = lax.axis_size("seq")
    count = lax.axis_size("dp") * seq_count
    bits = count.bit_length() - 1
    me = lax.axis_index("dp") * seq_count + lax.axis_index("seq")
    orders = color_orders(bits)
    local_rows = tokens.shape[0] // BLOCK
    all_rows = local_rows * seq_count
    columns = BLOCK // seq_count
    windows = all_rows // WIN_ROWS

    def to_columns(rows_array):
        w = rows_array.shape[-1]
        shaped = rows_array.reshape(local_rows, BLOCK, w)
        moved = lax.all_to_all(shaped, "seq", split_axis=1, concat_axis=0, tiled=True)
        return moved.reshape(all_rows * columns, w)

    def to_rows(column_array):
        w = column_array.shape[-1]
        shaped = column_array.reshape(all_rows, columns, w)
        moved = lax.all_to_all(shaped, "seq", split_axis=0, concat_axis=1, tiled=True)
        return moved.reshape(local_rows * BLOCK, w)

    def heads(flat):
        return flat.reshape(windows, WIN_ROWS, columns, HEADS, head_dim)

    gain_first = attn_gain.astype(WIDE)
    shift_first = attn_shift.astype(WIDE)
    gain_second = mlp_gain.astype(WIDE)
    shift_second = mlp_shift.astype(WIDE)

    tokens_col = to_columns(tokens)
    cotangent_col = to_columns(cotangent)

    group_segments = segment_ids.reshape(all_rows, BLOCK)
    my_segments = lax.dynamic_slice_in_dim(
        group_segments, lax.axis_index("seq") * columns, columns, 1
    )
    seg = jnp.transpose(my_segments.reshape(windows, WIN_ROWS, columns), (0, 2, 1))
    row_ids = jnp.arange(WIN_ROWS)
    causal = row_ids[None, :] <= row_ids[:, None]
    allowed = (seg[:, :, :, None] == seg[:, :, None, :]) & causal
    allowed = allowed[:, :, None]

    residual = tokens_col.astype(WIDE)
    first, first_scaled, first_inverse = norm_forward(residual, gain_first, shift_first)
    first_low = first.astype(NARROW)
    bias_all = jnp.concatenate(
        [query_bias.astype(WIDE), jnp.zeros((width,), WIDE), value_bias.astype(WIDE)]
    )
    projected = (jnp.dot(first_low, qkv_weight, preferred_element_type=WIDE) + bias_all).astype(
        NARROW
    )
    queries = heads(projected[:, :width])
    keys = heads(projected[:, width : 2 * width])
    values = heads(projected[:, 2 * width :])
    raw = jnp.einsum("wqchd,wkchd->wchqk", queries, keys, preferred_element_type=WIDE)
    logits = jnp.where(allowed, raw * scale, NEG_FILL)
    peak = jnp.max(logits, axis=-1, keepdims=True)
    total = jnp.sum(jnp.exp(logits - peak), axis=-1, keepdims=True)
    log_total = peak + jnp.log(total)
    probs = jnp.exp(logits - log_total)
    probs_low = probs.astype(NARROW)
    attended = jnp.einsum("wchqk,wkchd->wqchd", probs_low, values, preferred_element_type=WIDE)
    attended = attended.astype(NARROW).reshape(-1, width)
    branch = jnp.dot(attended, out_weight, preferred_element_type=WIDE) + out_bias.astype(WIDE)
    middle = residual + branch
    second, second_scaled, second_inverse = norm_forward(middle, gain_second, shift_second)
    second_low = second.astype(NARROW)
    hidden = jnp.dot(second_low, up_weight, preferred_element_type=WIDE) + up_bias.astype(WIDE)
    activated, gelu_pull = jax.vjp(gelu_tanh, hidden)
    activated_low = activated.astype(NARROW)
    mixed = jnp.dot(activated_low, down_weight, preferred_element_type=WIDE) + down_bias.astype(
        WIDE
    )
    output = to_rows((middle + mixed).astype(NARROW))

    grad_out = cotangent_col.astype(WIDE)
    grad_down_weight = reduced_weight(activated_low, cotangent_col, me, count, orders[:1])
    grad_down_bias = jnp.sum(grad_out, axis=0)
    grad_activated = jnp.einsum(
        "td,fd->tf", cotangent_col, down_weight, preferred_element_type=WIDE
    )
    grad_hidden = gelu_pull(grad_activated)[0].astype(NARROW)
    grad_up_bias = jnp.sum(grad_hidden, axis=0, dtype=WIDE)
    grad_up_weight = reduced_weight(second_low, grad_hidden, me, count, orders[1:2])
    grad_second = jnp.einsum("tf,df->td", grad_hidden, up_weight, preferred_element_type=WIDE)
    grad_middle_norm, grad_mlp_gain, grad_mlp_shift = norm_backward(
        grad_second, gain_second, second_scaled, second_inverse
    )
    grad_middle = grad_out + grad_middle_norm
    grad_branch = grad_middle.astype(NARROW)
    grad_out_bias = jnp.sum(grad_branch, axis=0, dtype=WIDE)
    grad_out_weight = reduced_weight(attended, grad_branch, me, count, orders[2:])
    grad_attended = jnp.einsum("te,de->td", grad_branch, out_weight, preferred_element_type=WIDE)
    grad_heads = heads(grad_attended.astype(NARROW))
    grad_values = jnp.einsum(
        "wchqk,wqchd->wkchd", probs_low, grad_heads, preferred_element_type=WIDE
    )
    grad_probs = jnp.einsum("wqchd,wkchd->wchqk", grad_heads, values, preferred_element_type=WIDE)
    grad_logits = (
        probs * (grad_probs - jnp.sum(probs * grad_probs, axis=-1, keepdims=True))
    ).astype(NARROW)
    grad_queries = (
        jnp.einsum("wchqk,wkchd->wqchd", grad_logits, keys, preferred_element_type=WIDE)
        * scale
    )
    grad_keys = (
        jnp.einsum("wchqk,wqchd->wkchd", grad_logits, queries, preferred_element_type=WIDE)
        * scale
    )
    grad_projected = jnp.concatenate(
        [
            grad_queries.astype(NARROW).reshape(-1, width),
            grad_keys.astype(NARROW).reshape(-1, width),
            grad_values.astype(NARROW).reshape(-1, width),
        ],
        axis=-1,
    )
    grad_query_bias = jnp.sum(grad_projected[:, :width], axis=0, dtype=WIDE)
    grad_value_bias = jnp.sum(grad_projected[:, 2 * width :], axis=0, dtype=WIDE)
    grad_qkv_weight = reduced_weight(first_low, grad_projected, me, count, orders)
    grad_first = jnp.einsum("te,de->td", grad_projected, qkv_weight, preferred_element_type=WIDE)
    grad_token_norm, grad_attn_gain, grad_attn_shift = norm_backward(
        grad_first, gain_first, first_scaled, first_inverse
    )
    grad_tokens = to_rows((grad_middle + grad_token_norm).astype(NARROW))

    vectors = (
        grad_attn_gain,
        grad_attn_shift,
        grad_query_bias,
        grad_value_bias,
        grad_out_bias,
        grad_mlp_gain,
        grad_mlp_shift,
        grad_up_bias,
        grad_down_bias,
    )
    packed = jnp.concatenate([v.reshape(count, -1) for v in vectors], axis=1)
    summed = halving(packed, orders[1], me, count)
    cuts = [0]
    for v in vectors:
        cuts.append(cuts[-1] + v.shape[0] // count)
    (
        grad_attn_gain,
        grad_attn_shift,
        grad_query_bias,
        grad_value_bias,
        grad_out_bias,
        grad_mlp_gain,
        grad_mlp_shift,
        grad_up_bias,
        grad_down_bias,
    ) = [summed[0, a:b] for a, b in zip(cuts[:-1], cuts[1:])]
    return (
        output,
        grad_tokens,
        grad_attn_gain,
        grad_attn_shift,
        grad_qkv_weight,
        grad_query_bias,
        grad_value_bias,
        grad_out_weight,
        grad_out_bias,
        grad_mlp_gain,
        grad_mlp_shift,
        grad_up_weight,
        grad_up_bias,
        grad_down_weight,
        grad_down_bias,
    )


def solution(mesh):
    placed = (
        P(("dp", "seq"), None),
        P("dp"),
        P(),
        P(),
        P(),
        P(),
        P(),
        P(),
        P(),
        P(),
        P(),
        P(),
        P(),
        P(),
        P(),
        P(("dp", "seq"), None),
    )
    return jax.shard_map(
        layer_body,
        mesh=mesh,
        in_specs=placed,
        out_specs=(
            P(("dp", "seq"), None),
            P(("dp", "seq"), None),
            P(("dp", "seq")),
            P(("dp", "seq")),
            P(("dp", "seq"), None),
            P(("dp", "seq")),
            P(("dp", "seq")),
            P(("dp", "seq"), None),
            P(("dp", "seq")),
            P(("dp", "seq")),
            P(("dp", "seq")),
            P(("dp", "seq"), None),
            P(("dp", "seq")),
            P(("dp", "seq"), None),
            P(("dp", "seq")),
        ),
        check_vma=False,
    )
```

```python
import jax
import jax.numpy as jnp
from jax import lax
from jax.sharding import PartitionSpec as P


HEADS = 16
BLOCK = 128
WIN_ROWS = 64


EPSILON = 1e-05
NEG_FILL = -1e30
WIDE = jnp.float32
NARROW = jnp.bfloat16
AXES = ("dp", "seq")
COLOR_FRACTIONS = (0.375, 0.375, 0.25)


def gelu_tanh(values):
    return (
        0.5
        * values
        * (1.0 + jnp.tanh(0.7978845608028654 * (values + 0.044715 * values * values * values)))
    )


def norm_forward(values, gain, shift):
    center = values - jnp.mean(values, axis=-1, keepdims=True)
    inverse = lax.rsqrt(jnp.mean(center * center, axis=-1, keepdims=True) + EPSILON)
    scaled = center * inverse
    return (scaled * gain + shift, scaled, inverse)


def norm_backward(upstream, gain, scaled, inverse):
    weighted = upstream * gain
    inner = (
        weighted
        - jnp.mean(weighted, axis=-1, keepdims=True)
        - scaled * jnp.mean(weighted * scaled, axis=-1, keepdims=True)
    )
    return (inverse * inner, jnp.sum(upstream * scaled, axis=0), jnp.sum(upstream, axis=0))


def color_orders(bits):
    if bits == 5:
        return [[0, 4, 1, 2, 3], [0, 1, 2, 4, 3], [0, 2, 4, 1, 3]]
    rest = list(range(1, bits))
    if not rest:
        return [[0]]
    starts = [len(rest) - 1, 0, 1]
    return [[0] + rest[s % len(rest):] + rest[: s % len(rest)] for s in starts]


def halving(part, order, me, count):
    bits = len(order)
    rows, cols = part.shape
    buf = part.reshape((2,) * bits + (rows // count, cols))
    left = list(range(bits - 1, -1, -1))
    for bit in order:
        axis = left.index(bit)
        mine = (me >> bit) & 1
        keep = lax.dynamic_index_in_dim(buf, mine, axis, keepdims=False)
        send = lax.dynamic_index_in_dim(buf, 1 - mine, axis, keepdims=False).astype(NARROW)
        got = lax.ppermute(send, AXES, [(i, i ^ (1 << bit)) for i in range(count)])
        buf = keep.astype(WIDE) + got.astype(WIDE)
        left.pop(axis)
    return buf.reshape(rows // count, cols)


def color_cuts(cols):
    cuts = [0]
    for fraction in COLOR_FRACTIONS[:-1]:
        cuts.append(cuts[-1] + max(128, int(round(cols * fraction / 128)) * 128))
    cuts.append(cols)
    return cuts


def reduced_weight(lhs, rhs, me, count, orders):
    cols = rhs.shape[1]
    cuts = color_cuts(cols) if len(orders) > 1 else [0, cols]
    pieces = []
    for a, b, order in zip(cuts[:-1], cuts[1:], orders):
        partial = jnp.einsum("tr,tc->rc", lhs, rhs[:, a:b], preferred_element_type=WIDE)
        pieces.append(halving(partial, order, me, count))
    return pieces[0] if len(pieces) == 1 else jnp.concatenate(pieces, axis=1)


def layer_body(
    tokens,
    segment_ids,
    attn_gain,
    attn_shift,
    qkv_weight,
    query_bias,
    value_bias,
    out_weight,
    out_bias,
    mlp_gain,
    mlp_shift,
    up_weight,
    up_bias,
    down_weight,
    down_bias,
    cotangent,
):
    width = tokens.shape[1]
    head_dim = width // HEADS
    scale = head_dim ** (-0.5)
    seq_count = lax.axis_size("seq")
    count = lax.axis_size("dp") * seq_count
    bits = count.bit_length() - 1
    me = lax.axis_index("dp") * seq_count + lax.axis_index("seq")
    orders = color_orders(bits)
    local_rows = tokens.shape[0] // BLOCK
    all_rows = local_rows * seq_count
    columns = BLOCK // seq_count
    windows = all_rows // WIN_ROWS

    def to_columns(rows_array):
        w = rows_array.shape[-1]
        shaped = rows_array.reshape(local_rows, BLOCK, w)
        moved = lax.all_to_all(shaped, "seq", split_axis=1, concat_axis=0, tiled=True)
        return moved.reshape(all_rows * columns, w)

    def to_rows(column_array):
        w = column_array.shape[-1]
        shaped = column_array.reshape(all_rows, columns, w)
        moved = lax.all_to_all(shaped, "seq", split_axis=0, concat_axis=1, tiled=True)
        return moved.reshape(local_rows * BLOCK, w)

    def heads(flat):
        return flat.reshape(windows, WIN_ROWS, columns, HEADS, head_dim)

    gain_first = attn_gain.astype(WIDE)
    shift_first = attn_shift.astype(WIDE)
    gain_second = mlp_gain.astype(WIDE)
    shift_second = mlp_shift.astype(WIDE)

    tokens_col = to_columns(tokens)
    cotangent_col = to_columns(cotangent)

    group_segments = segment_ids.reshape(all_rows, BLOCK)
    my_segments = lax.dynamic_slice_in_dim(
        group_segments, lax.axis_index("seq") * columns, columns, 1
    )
    seg = jnp.transpose(my_segments.reshape(windows, WIN_ROWS, columns), (0, 2, 1))
    row_ids = jnp.arange(WIN_ROWS)
    causal = row_ids[None, :] <= row_ids[:, None]
    allowed = (seg[:, :, :, None] == seg[:, :, None, :]) & causal
    allowed = allowed[:, :, None]

    residual = tokens_col.astype(WIDE)
    first, first_scaled, first_inverse = norm_forward(residual, gain_first, shift_first)
    first_low = first.astype(NARROW)
    bias_all = jnp.concatenate(
        [query_bias.astype(WIDE), jnp.zeros((width,), WIDE), value_bias.astype(WIDE)]
    )
    projected = (jnp.dot(first_low, qkv_weight, preferred_element_type=WIDE) + bias_all).astype(
        NARROW
    )
    queries = heads(projected[:, :width])
    keys = heads(projected[:, width : 2 * width])
    values = heads(projected[:, 2 * width :])
    raw = jnp.einsum("wqchd,wkchd->wchqk", queries, keys, preferred_element_type=WIDE)
    logits = jnp.where(allowed, raw * scale, NEG_FILL)
    peak = jnp.max(logits, axis=-1, keepdims=True)
    total = jnp.sum(jnp.exp(logits - peak), axis=-1, keepdims=True)
    log_total = peak + jnp.log(total)
    probs = jnp.exp(logits - log_total)
    probs_low = probs.astype(NARROW)
    attended = jnp.einsum("wchqk,wkchd->wqchd", probs_low, values, preferred_element_type=WIDE)
    attended = attended.astype(NARROW).reshape(-1, width)
    branch = jnp.dot(attended, out_weight, preferred_element_type=WIDE) + out_bias.astype(WIDE)
    middle = residual + branch
    second, second_scaled, second_inverse = norm_forward(middle, gain_second, shift_second)
    second_low = second.astype(NARROW)
    hidden = jnp.dot(second_low, up_weight, preferred_element_type=WIDE) + up_bias.astype(WIDE)
    activated, gelu_pull = jax.vjp(gelu_tanh, hidden)
    activated_low = activated.astype(NARROW)
    mixed = jnp.dot(activated_low, down_weight, preferred_element_type=WIDE) + down_bias.astype(
        WIDE
    )
    output = to_rows((middle + mixed).astype(NARROW))

    grad_out = cotangent_col.astype(WIDE)
    grad_down_weight = reduced_weight(activated_low, cotangent_col, me, count, orders)
    grad_down_bias = jnp.sum(grad_out, axis=0)
    grad_activated = jnp.einsum(
        "td,fd->tf", cotangent_col, down_weight, preferred_element_type=WIDE
    )
    grad_hidden = gelu_pull(grad_activated)[0].astype(NARROW)
    grad_up_bias = jnp.sum(grad_hidden, axis=0, dtype=WIDE)
    grad_up_weight = reduced_weight(second_low, grad_hidden, me, count, orders)
    grad_second = jnp.einsum("tf,df->td", grad_hidden, up_weight, preferred_element_type=WIDE)
    grad_middle_norm, grad_mlp_gain, grad_mlp_shift = norm_backward(
        grad_second, gain_second, second_scaled, second_inverse
    )
    grad_middle = grad_out + grad_middle_norm
    grad_branch = grad_middle.astype(NARROW)
    grad_out_bias = jnp.sum(grad_branch, axis=0, dtype=WIDE)
    grad_out_weight = reduced_weight(attended, grad_branch, me, count, orders[2:])
    grad_attended = jnp.einsum("te,de->td", grad_branch, out_weight, preferred_element_type=WIDE)
    grad_heads = heads(grad_attended.astype(NARROW))
    grad_values = jnp.einsum(
        "wchqk,wqchd->wkchd", probs_low, grad_heads, preferred_element_type=WIDE
    )
    grad_probs = jnp.einsum("wqchd,wkchd->wchqk", grad_heads, values, preferred_element_type=WIDE)
    grad_logits = (
        probs * (grad_probs - jnp.sum(probs * grad_probs, axis=-1, keepdims=True))
    ).astype(NARROW)
    grad_queries = (
        jnp.einsum("wchqk,wkchd->wqchd", grad_logits, keys, preferred_element_type=WIDE)
        * scale
    )
    grad_keys = (
        jnp.einsum("wchqk,wqchd->wkchd", grad_logits, queries, preferred_element_type=WIDE)
        * scale
    )
    grad_projected = jnp.concatenate(
        [
            grad_queries.astype(NARROW).reshape(-1, width),
            grad_keys.astype(NARROW).reshape(-1, width),
            grad_values.astype(NARROW).reshape(-1, width),
        ],
        axis=-1,
    )
    grad_query_bias = jnp.sum(grad_projected[:, :width], axis=0, dtype=WIDE)
    grad_value_bias = jnp.sum(grad_projected[:, 2 * width :], axis=0, dtype=WIDE)
    grad_qkv_weight = reduced_weight(first_low, grad_projected, me, count, orders)
    grad_first = jnp.einsum("te,de->td", grad_projected, qkv_weight, preferred_element_type=WIDE)
    grad_token_norm, grad_attn_gain, grad_attn_shift = norm_backward(
        grad_first, gain_first, first_scaled, first_inverse
    )
    grad_tokens = to_rows((grad_middle + grad_token_norm).astype(NARROW))

    vectors = (
        grad_attn_gain,
        grad_attn_shift,
        grad_query_bias,
        grad_value_bias,
        grad_out_bias,
        grad_mlp_gain,
        grad_mlp_shift,
        grad_up_bias,
        grad_down_bias,
    )
    packed = jnp.concatenate([v.reshape(count, -1) for v in vectors], axis=1)
    summed = halving(packed, orders[1], me, count)
    cuts = [0]
    for v in vectors:
        cuts.append(cuts[-1] + v.shape[0] // count)
    (
        grad_attn_gain,
        grad_attn_shift,
        grad_query_bias,
        grad_value_bias,
        grad_out_bias,
        grad_mlp_gain,
        grad_mlp_shift,
        grad_up_bias,
        grad_down_bias,
    ) = [summed[0, a:b] for a, b in zip(cuts[:-1], cuts[1:])]
    return (
        output,
        grad_tokens,
        grad_attn_gain,
        grad_attn_shift,
        grad_qkv_weight,
        grad_query_bias,
        grad_value_bias,
        grad_out_weight,
        grad_out_bias,
        grad_mlp_gain,
        grad_mlp_shift,
        grad_up_weight,
        grad_up_bias,
        grad_down_weight,
        grad_down_bias,
    )


def solution(mesh):
    placed = (
        P(("dp", "seq"), None),
        P("dp"),
        P(),
        P(),
        P(),
        P(),
        P(),
        P(),
        P(),
        P(),
        P(),
        P(),
        P(),
        P(),
        P(),
        P(("dp", "seq"), None),
    )
    return jax.shard_map(
        layer_body,
        mesh=mesh,
        in_specs=placed,
        out_specs=(
            P(("dp", "seq"), None),
            P(("dp", "seq"), None),
            P(("dp", "seq")),
            P(("dp", "seq")),
            P(("dp", "seq"), None),
            P(("dp", "seq")),
            P(("dp", "seq")),
            P(("dp", "seq"), None),
            P(("dp", "seq")),
            P(("dp", "seq")),
            P(("dp", "seq")),
            P(("dp", "seq"), None),
            P(("dp", "seq")),
            P(("dp", "seq"), None),
            P(("dp", "seq")),
        ),
        check_vma=False,
    )
```

```python
import functools

import jax
import jax.numpy as jnp
from jax import lax
from jax.experimental import pallas as pl
from jax.sharding import PartitionSpec as P


HEADS = 16
BLOCK = 128
WIN_ROWS = 64


EPSILON = 1e-05
NEG_FILL = -1e30
WIDE = jnp.float32
NARROW = jnp.bfloat16
AXES = ("dp", "seq")
COLOR_FRACTIONS = (0.375, 0.375, 0.25)


def _masks(segr_ref, segc_ref, rows):
    i = lax.broadcasted_iota(jnp.int32, (rows, rows), 0)
    j = lax.broadcasted_iota(jnp.int32, (rows, rows), 1)
    allowed = (segr_ref[0] == segc_ref[0]) & (j <= i)
    lane = lax.broadcasted_iota(jnp.int32, (1, 128), 1)
    return allowed, lane


def _probs(qh, k2, allowed, scale):
    raw = lax.dot_general(qh, k2, (((1,), (1,)), ((), ())), preferred_element_type=jnp.float32)
    logits = jnp.where(allowed, raw * scale, NEG_FILL)
    peak = jnp.max(logits, axis=-1, keepdims=True)
    total = jnp.sum(jnp.exp(logits - peak), axis=-1, keepdims=True)
    return jnp.exp(logits - (peak + jnp.log(total)))


def attn_fwd_kernel(qkv_ref, segr_ref, segc_ref, out_ref, *, width, scale):
    rows = out_ref.shape[1]
    head_dim = width // HEADS
    allowed, lane = _masks(segr_ref, segc_ref, rows)
    for p in range(width // 128):
        q2 = qkv_ref[0, :, p * 128:(p + 1) * 128]
        k2 = qkv_ref[0, :, width + p * 128:width + (p + 1) * 128]
        v2 = qkv_ref[0, :, 2 * width + p * 128:2 * width + (p + 1) * 128]
        out = jnp.zeros((rows, 128), jnp.float32)
        for h in range(128 // head_dim):
            mine = (lane >= h * head_dim) & (lane < (h + 1) * head_dim)
            qh = jnp.where(mine, q2, jnp.zeros_like(q2))
            vh = jnp.where(mine, v2, jnp.zeros_like(v2))
            probs_low = _probs(qh, k2, allowed, scale).astype(jnp.bfloat16)
            out = out + jnp.dot(probs_low, vh, preferred_element_type=jnp.float32)
        out_ref[0, :, p * 128:(p + 1) * 128] = out.astype(out_ref.dtype)


def attn_bwd_kernel(qkv_ref, go_ref, segr_ref, segc_ref, g_ref, *, width, scale):
    rows = go_ref.shape[1]
    head_dim = width // HEADS
    allowed, lane = _masks(segr_ref, segc_ref, rows)
    for p in range(width // 128):
        q2 = qkv_ref[0, :, p * 128:(p + 1) * 128]
        k2 = qkv_ref[0, :, width + p * 128:width + (p + 1) * 128]
        v2 = qkv_ref[0, :, 2 * width + p * 128:2 * width + (p + 1) * 128]
        go2 = go_ref[0, :, p * 128:(p + 1) * 128]
        gq = jnp.zeros((rows, 128), jnp.float32)
        gk = jnp.zeros((rows, 128), jnp.float32)
        gv = jnp.zeros((rows, 128), jnp.float32)
        for h in range(128 // head_dim):
            mine = (lane >= h * head_dim) & (lane < (h + 1) * head_dim)
            qh = jnp.where(mine, q2, jnp.zeros_like(q2))
            kh = jnp.where(mine, k2, jnp.zeros_like(k2))
            goh = jnp.where(mine, go2, jnp.zeros_like(go2))
            probs = _probs(qh, k2, allowed, scale)
            probs_low_t = probs.T.astype(jnp.bfloat16)
            gv = gv + jnp.dot(probs_low_t, goh, preferred_element_type=jnp.float32)
            grad_probs = lax.dot_general(goh, v2, (((1,), (1,)), ((), ())), preferred_element_type=jnp.float32)
            inner = probs * (grad_probs - jnp.sum(probs * grad_probs, axis=-1, keepdims=True))
            gl = inner.astype(jnp.bfloat16)
            gl_t = inner.T.astype(jnp.bfloat16)
            gq = gq + jnp.dot(gl, kh, preferred_element_type=jnp.float32) * scale
            gk = gk + jnp.dot(gl_t, qh, preferred_element_type=jnp.float32) * scale
        g_ref[0, :, p * 128:(p + 1) * 128] = gq.astype(g_ref.dtype)
        g_ref[0, :, width + p * 128:width + (p + 1) * 128] = gk.astype(g_ref.dtype)
        g_ref[0, :, 2 * width + p * 128:2 * width + (p + 1) * 128] = gv.astype(g_ref.dtype)


def attention_forward(qkv, segr, segc, scale, interpret=False):
    groups, rows, three = qkv.shape
    width = three // 3
    return pl.pallas_call(
        functools.partial(attn_fwd_kernel, width=width, scale=scale),
        out_shape=jax.ShapeDtypeStruct((groups, rows, width), jnp.bfloat16),
        grid=(groups,),
        in_specs=[pl.BlockSpec((1, rows, three), lambda g: (g, 0, 0)),
                  pl.BlockSpec((1, rows, 1), lambda g: (g, 0, 0)),
                  pl.BlockSpec((1, 1, rows), lambda g: (g, 0, 0))],
        out_specs=pl.BlockSpec((1, rows, width), lambda g: (g, 0, 0)),
        cost_estimate=pl.CostEstimate(
            flops=4 * groups * rows * rows * 128 * width // 64 * 1,
            transcendentals=groups * HEADS * rows * rows,
            bytes_accessed=groups * rows * 4 * width * 2,
        ),
        interpret=interpret,
    )(qkv, segr, segc)


def attention_backward(qkv, go, segr, segc, scale, interpret=False):
    groups, rows, three = qkv.shape
    width = three // 3
    return pl.pallas_call(
        functools.partial(attn_bwd_kernel, width=width, scale=scale),
        out_shape=jax.ShapeDtypeStruct((groups, rows, three), jnp.bfloat16),
        grid=(groups,),
        in_specs=[pl.BlockSpec((1, rows, three), lambda g: (g, 0, 0)),
                  pl.BlockSpec((1, rows, width), lambda g: (g, 0, 0)),
                  pl.BlockSpec((1, rows, 1), lambda g: (g, 0, 0)),
                  pl.BlockSpec((1, 1, rows), lambda g: (g, 0, 0))],
        out_specs=pl.BlockSpec((1, rows, three), lambda g: (g, 0, 0)),
        cost_estimate=pl.CostEstimate(
            flops=12 * groups * rows * rows * 128 * width // 64,
            transcendentals=groups * HEADS * rows * rows,
            bytes_accessed=groups * rows * 7 * width * 2,
        ),
        interpret=interpret,
    )(qkv, go, segr, segc)


def gelu_tanh(values):
    return (
        0.5
        * values
        * (1.0 + jnp.tanh(0.7978845608028654 * (values + 0.044715 * values * values * values)))
    )


def norm_forward(values, gain, shift):
    center = values - jnp.mean(values, axis=-1, keepdims=True)
    inverse = lax.rsqrt(jnp.mean(center * center, axis=-1, keepdims=True) + EPSILON)
    scaled = center * inverse
    return (scaled * gain + shift, scaled, inverse)


def norm_backward(upstream, gain, scaled, inverse):
    weighted = upstream * gain
    inner = (
        weighted
        - jnp.mean(weighted, axis=-1, keepdims=True)
        - scaled * jnp.mean(weighted * scaled, axis=-1, keepdims=True)
    )
    return (inverse * inner, jnp.sum(upstream * scaled, axis=0), jnp.sum(upstream, axis=0))


def color_orders(bits):
    if bits == 5:
        return [[0, 4, 1, 2, 3], [0, 1, 2, 4, 3], [0, 2, 4, 1, 3]]
    rest = list(range(1, bits))
    if not rest:
        return [[0]]
    starts = [len(rest) - 1, 0, 1]
    return [[0] + rest[s % len(rest):] + rest[: s % len(rest)] for s in starts]


def halving(part, order, me, count):
    bits = len(order)
    rows, cols = part.shape
    buf = part.reshape((2,) * bits + (rows // count, cols))
    left = list(range(bits - 1, -1, -1))
    for bit in order:
        axis = left.index(bit)
        mine = (me >> bit) & 1
        keep = lax.dynamic_index_in_dim(buf, mine, axis, keepdims=False)
        send = lax.dynamic_index_in_dim(buf, 1 - mine, axis, keepdims=False).astype(NARROW)
        got = lax.ppermute(send, AXES, [(i, i ^ (1 << bit)) for i in range(count)])
        buf = keep.astype(WIDE) + got.astype(WIDE)
        left.pop(axis)
    return buf.reshape(rows // count, cols)


def color_cuts(cols):
    cuts = [0]
    for fraction in COLOR_FRACTIONS[:-1]:
        cuts.append(cuts[-1] + max(128, int(round(cols * fraction / 128)) * 128))
    cuts.append(cols)
    return cuts


def reduced_weight(lhs, rhs, me, count, orders):
    cols = rhs.shape[1]
    cuts = color_cuts(cols) if len(orders) > 1 else [0, cols]
    pieces = []
    for a, b, order in zip(cuts[:-1], cuts[1:], orders):
        partial = jnp.einsum("tr,tc->rc", lhs, rhs[:, a:b], preferred_element_type=WIDE)
        pieces.append(halving(partial, order, me, count))
    return pieces[0] if len(pieces) == 1 else jnp.concatenate(pieces, axis=1)


def layer_body(
    tokens,
    segment_ids,
    attn_gain,
    attn_shift,
    qkv_weight,
    query_bias,
    value_bias,
    out_weight,
    out_bias,
    mlp_gain,
    mlp_shift,
    up_weight,
    up_bias,
    down_weight,
    down_bias,
    cotangent,
):
    width = tokens.shape[1]
    head_dim = width // HEADS
    scale = head_dim ** (-0.5)
    seq_count = lax.axis_size("seq")
    count = lax.axis_size("dp") * seq_count
    bits = count.bit_length() - 1
    me = lax.axis_index("dp") * seq_count + lax.axis_index("seq")
    orders = color_orders(bits)
    local_rows = tokens.shape[0] // BLOCK
    all_rows = local_rows * seq_count
    columns = BLOCK // seq_count
    windows = all_rows // WIN_ROWS

    def to_columns(rows_array):
        w = rows_array.shape[-1]
        shaped = jnp.transpose(rows_array.reshape(local_rows, BLOCK, w), (1, 0, 2))
        moved = lax.all_to_all(shaped, "seq", split_axis=0, concat_axis=1, tiled=True)
        return moved.reshape(columns * all_rows, w)

    def to_rows(column_array):
        w = column_array.shape[-1]
        shaped = column_array.reshape(columns, all_rows, w)
        moved = lax.all_to_all(shaped, "seq", split_axis=1, concat_axis=0, tiled=True)
        return jnp.transpose(moved, (1, 0, 2)).reshape(local_rows * BLOCK, w)

    def groups(flat):
        return flat.reshape(columns * windows, WIN_ROWS, flat.shape[-1])

    gain_first = attn_gain.astype(WIDE)
    shift_first = attn_shift.astype(WIDE)
    gain_second = mlp_gain.astype(WIDE)
    shift_second = mlp_shift.astype(WIDE)

    tokens_col = to_columns(tokens)
    cotangent_col = to_columns(cotangent)

    group_segments = segment_ids.reshape(all_rows, BLOCK)
    my_segments = lax.dynamic_slice_in_dim(
        group_segments, lax.axis_index("seq") * columns, columns, 1
    )
    seg = jnp.transpose(my_segments).reshape(columns * windows, WIN_ROWS)
    seg_rows = seg[:, :, None]
    seg_cols = seg[:, None, :]

    residual = tokens_col.astype(WIDE)
    first, first_scaled, first_inverse = norm_forward(residual, gain_first, shift_first)
    first_low = first.astype(NARROW)
    bias_all = jnp.concatenate(
        [query_bias.astype(WIDE), jnp.zeros((width,), WIDE), value_bias.astype(WIDE)]
    )
    projected = (jnp.dot(first_low, qkv_weight, preferred_element_type=WIDE) + bias_all).astype(
        NARROW
    )
    attended = attention_forward(groups(projected), seg_rows, seg_cols, scale).reshape(-1, width)
    branch = jnp.dot(attended, out_weight, preferred_element_type=WIDE) + out_bias.astype(WIDE)
    middle = residual + branch
    second, second_scaled, second_inverse = norm_forward(middle, gain_second, shift_second)
    second_low = second.astype(NARROW)
    hidden = jnp.dot(second_low, up_weight, preferred_element_type=WIDE) + up_bias.astype(WIDE)
    activated, gelu_pull = jax.vjp(gelu_tanh, hidden)
    activated_low = activated.astype(NARROW)
    mixed = jnp.dot(activated_low, down_weight, preferred_element_type=WIDE) + down_bias.astype(
        WIDE
    )
    output = to_rows((middle + mixed).astype(NARROW))

    grad_out = cotangent_col.astype(WIDE)
    grad_down_weight = reduced_weight(activated_low, cotangent_col, me, count, orders)
    grad_down_bias = jnp.sum(grad_out, axis=0)
    grad_activated = jnp.einsum(
        "td,fd->tf", cotangent_col, down_weight, preferred_element_type=WIDE
    )
    grad_hidden = gelu_pull(grad_activated)[0].astype(NARROW)
    grad_up_bias = jnp.sum(grad_hidden, axis=0, dtype=WIDE)
    grad_up_weight = reduced_weight(second_low, grad_hidden, me, count, orders)
    grad_second = jnp.einsum("tf,df->td", grad_hidden, up_weight, preferred_element_type=WIDE)
    grad_middle_norm, grad_mlp_gain, grad_mlp_shift = norm_backward(
        grad_second, gain_second, second_scaled, second_inverse
    )
    grad_middle = grad_out + grad_middle_norm
    grad_branch = grad_middle.astype(NARROW)
    grad_out_bias = jnp.sum(grad_branch, axis=0, dtype=WIDE)
    grad_out_weight = reduced_weight(attended, grad_branch, me, count, orders[2:])
    grad_attended = jnp.einsum("te,de->td", grad_branch, out_weight, preferred_element_type=WIDE)
    grad_projected = attention_backward(
        groups(projected), groups(grad_attended.astype(NARROW)), seg_rows, seg_cols, scale
    ).reshape(-1, 3 * width)
    grad_query_bias = jnp.sum(grad_projected[:, :width], axis=0, dtype=WIDE)
    grad_value_bias = jnp.sum(grad_projected[:, 2 * width :], axis=0, dtype=WIDE)
    grad_qkv_weight = reduced_weight(first_low, grad_projected, me, count, orders)
    grad_first = jnp.einsum("te,de->td", grad_projected, qkv_weight, preferred_element_type=WIDE)
    grad_token_norm, grad_attn_gain, grad_attn_shift = norm_backward(
        grad_first, gain_first, first_scaled, first_inverse
    )
    grad_tokens = to_rows((grad_middle + grad_token_norm).astype(NARROW))

    vectors = (
        grad_attn_gain,
        grad_attn_shift,
        grad_query_bias,
        grad_value_bias,
        grad_out_bias,
        grad_mlp_gain,
        grad_mlp_shift,
        grad_up_bias,
        grad_down_bias,
    )
    packed = jnp.concatenate([v.reshape(count, -1) for v in vectors], axis=1)
    summed = halving(packed, orders[1], me, count)
    cuts = [0]
    for v in vectors:
        cuts.append(cuts[-1] + v.shape[0] // count)
    (
        grad_attn_gain,
        grad_attn_shift,
        grad_query_bias,
        grad_value_bias,
        grad_out_bias,
        grad_mlp_gain,
        grad_mlp_shift,
        grad_up_bias,
        grad_down_bias,
    ) = [summed[0, a:b] for a, b in zip(cuts[:-1], cuts[1:])]
    return (
        output,
        grad_tokens,
        grad_attn_gain,
        grad_attn_shift,
        grad_qkv_weight,
        grad_query_bias,
        grad_value_bias,
        grad_out_weight,
        grad_out_bias,
        grad_mlp_gain,
        grad_mlp_shift,
        grad_up_weight,
        grad_up_bias,
        grad_down_weight,
        grad_down_bias,
    )


def solution(mesh):
    placed = (
        P(("dp", "seq"), None),
        P("dp"),
        P(),
        P(),
        P(),
        P(),
        P(),
        P(),
        P(),
        P(),
        P(),
        P(),
        P(),
        P(),
        P(),
        P(("dp", "seq"), None),
    )
    return jax.shard_map(
        layer_body,
        mesh=mesh,
        in_specs=placed,
        out_specs=(
            P(("dp", "seq"), None),
            P(("dp", "seq"), None),
            P(("dp", "seq")),
            P(("dp", "seq")),
            P(("dp", "seq"), None),
            P(("dp", "seq")),
            P(("dp", "seq")),
            P(("dp", "seq"), None),
            P(("dp", "seq")),
            P(("dp", "seq")),
            P(("dp", "seq")),
            P(("dp", "seq"), None),
            P(("dp", "seq")),
            P(("dp", "seq"), None),
            P(("dp", "seq")),
        ),
        check_vma=False,
    )
```
